256 devices in a mesh: chan: 64 (over z, y_hi, x), win: 4 (over y_lo, core).
Axes of the slice: x: 4, y: 4 (y_hi: 2, y_lo: 2; y = y_hi * 2 + y_lo), z: 8, core: 2. Of those that a mesh axis runs over, the one named last changes fastest.
Arguments:
- traces: float32 [8, 2048, 2048], P('win', 'chan'), may hold values from -200 to 200
- quality: int32 [8, 2048], P('win', 'chan'), may hold values 0 or 1
Outputs:
- correlations: bfloat16 [2048, 2048, 128], P('chan', 'win')
The draws below stay inside these ranges and needn't reach their ends.
Inputs may be any that keep to these rules, and one draw needn't show every extreme that they name: `quality`: 1 marks a usable window of a channel.
All inputs are finite; a program needn't handle non-finite values. No bound on the sum of `quality` on one device may be relied on, other than what follows from the above.
Results may differ from the reference program's by a relative error of at most 0.008.
Values may be sent and summed in bfloat16 or wider, within the bound.
No kernel may reach another device: no remote copies, remote signals or barrier semaphores. Data moves between devices by JAX's collectives and lax.ppermute only.
A program may use at most 128 MiB of HBM per device.

```python
import math
import jax
import jax.numpy as jnp
from jax import lax

C = 2048
WIN_DEV = 2
WINDOWS = 8
SEGS = 8
NFFT = 256
F = 128
BAND = 8
LAGS = 128
N_WIN = 4


def draw_traces(key, part):
    length = SEGS * NFFT
    scale_key, noise_key, bin_key, amp_key, phase_key = jax.random.split(key, 5)
    spread = jnp.exp(jax.random.uniform(scale_key, (WINDOWS, C, 1), jnp.float32, 0.0, jnp.log(10.0)))
    noise_part = jnp.clip(jax.random.normal(noise_key, (WINDOWS, C, length), jnp.float32), -5.0, 5.0)
    sample_index = jnp.arange(length, dtype=jnp.int32)
    tone_bins = jax.random.randint(bin_key, (3, C, 1), 1, F + 1)
    amplitudes = jax.random.uniform(amp_key, (3, 1, C, 1), jnp.float32, 0.5, 3.0)
    offsets = jax.random.uniform(phase_key, (3, WINDOWS, C, 1), jnp.float32, -jnp.pi, jnp.pi)
    signal = noise_part
    for tone_number in range(3):
        angles = 2.0 * jnp.pi / NFFT * (tone_bins[tone_number] * sample_index[None, :] % NFFT).astype(jnp.float32)
        signal = signal + amplitudes[tone_number] * jnp.cos(angles[None, :, :] + offsets[tone_number])
    return spread * signal


def place_ends(array, own_key, smallest, high):
    longest = array.shape.index(max(array.shape))
    spots = []
    for shift in (0, 1):
        where = [jax.random.randint(jax.random.fold_in(own_key, axis), (), 0, length) for axis, length in enumerate(array.shape)]
        where[longest] = (where[longest] + shift) % array.shape[longest]
        spots.append(tuple(where))
    return array.at[spots[0]].set(smallest).at[spots[1]].set(high)


def setup_inputs(seed: int = 0) -> dict:
    seeds = jax.random.split(jax.random.key(seed), 3)
    traces = draw_traces(jax.random.fold_in(seeds[2], 71), 0)
    quality = place_ends((jax.random.randint(seeds[1], (WINDOWS, C), 0, 4) < 3).astype(jnp.int32), jax.random.fold_in(seeds[1], 1), 0, 1)
    return dict(traces=traces, quality=quality)


epsilon = 1e-06
column_block = 512

def forward_table():
    sample_index = jnp.arange(NFFT, dtype=jnp.int32)[:, None]
    bin_index = jnp.arange(1, F + 1, dtype=jnp.int32)[None, :]
    angles = 2.0 * jnp.pi / NFFT * (sample_index * bin_index % NFFT).astype(jnp.float32)
    norm_scale = 1.0 / math.sqrt(NFFT)
    return jnp.concatenate([jnp.cos(angles), -jnp.sin(angles)], axis=1) * norm_scale

def lag_kernel(window_total):
    bin_index = jnp.arange(1, F + 1, dtype=jnp.int32)[:, None]
    lag_shift = jnp.arange(LAGS, dtype=jnp.int32)[None, :] - LAGS // 2
    angles = 2.0 * jnp.pi / NFFT * (bin_index * lag_shift % NFFT).astype(jnp.float32)
    norm_scale = 2.0 / math.sqrt(F * SEGS * window_total)
    return jnp.stack([jnp.cos(angles) * norm_scale, -jnp.sin(angles) * norm_scale]).astype(jnp.bfloat16)

def whiten(traces, quality):
    win_count, channels = (traces.shape[0], traces.shape[1])
    segments = traces.reshape(win_count, channels, SEGS, NFFT)
    spectrum = jnp.dot(segments, forward_table(), precision=lax.Precision.HIGHEST)
    real_part = spectrum[..., :F]
    imag_part = spectrum[..., F:]
    power_sum = (real_part * real_part + imag_part * imag_part).reshape(win_count, channels, SEGS, F // BAND, BAND)
    amplitude = jnp.sqrt(lax.optimization_barrier(jnp.mean(power_sum, axis=(2, 4))) + epsilon)
    factor = quality.astype(jnp.float32)[:, :, None] / amplitude
    factor = jnp.repeat(factor, BAND, axis=2)[:, :, None, :]
    stacked_parts = jnp.stack([real_part * factor, imag_part * factor], axis=0)
    stacked_parts = jnp.transpose(stacked_parts, (2, 0, 1, 3, 4)).reshape(channels, 2 * win_count * SEGS, F)
    return stacked_parts.astype(jnp.bfloat16)

def rotate(spectra):
    middle = spectra.shape[1] // 2
    return jnp.concatenate([spectra[:, middle:], -spectra[:, :middle]], axis=1)

def block_lags(stacked, theirs, kernel):
    cross_part = jnp.einsum('iwk,jwk->ijk', stacked.astype(jnp.float32), theirs.astype(jnp.float32)).astype(jnp.bfloat16)
    cross_part = cross_part.reshape(2, stacked.shape[0] // 2, theirs.shape[0], cross_part.shape[-1])
    return jnp.einsum('pijk,pkt->jit', cross_part.astype(jnp.float32), kernel.astype(jnp.float32))

def pair_lags(stacked, theirs, kernel):
    columns = theirs.shape[0]
    if columns > column_block and columns % column_block == 0:
        pieces = theirs.reshape(columns // column_block, column_block, theirs.shape[1], theirs.shape[2])
        lag_tiles = lax.map(lambda column_piece: block_lags(stacked, column_piece, kernel), pieces)
        return lag_tiles.reshape(columns, lag_tiles.shape[2], lag_tiles.shape[3])
    return block_lags(stacked, theirs, kernel)

def reference(traces, quality):
    kernel = lag_kernel(WINDOWS)
    groups = []
    for window_group in range(N_WIN):
        first_window = window_group * WIN_DEV
        groups.append(whiten(traces[first_window:first_window + WIN_DEV], quality[first_window:first_window + WIN_DEV]))
    spectra = jnp.stack(groups)
    row_count = math.gcd(C, 64)

    def row_block(row_start):
        running = jnp.zeros((C, row_count, LAGS), jnp.float32)
        for window_group in range(N_WIN):
            own_rows = lax.dynamic_slice_in_dim(spectra[window_group], row_start, row_count, 0)
            stacked = jnp.concatenate([own_rows, rotate(own_rows)], axis=0)
            rounded = pair_lags(stacked, spectra[window_group], kernel).astype(jnp.bfloat16)
            rounded = lax.optimization_barrier(rounded)
            running = running + rounded.astype(jnp.float32)
        return running.astype(jnp.bfloat16)
    starts = jnp.arange(0, C, row_count, dtype=jnp.int32)
    blocks = lax.map(row_block, starts)
    return jnp.transpose(blocks, (0, 2, 1, 3)).reshape(C, C, LAGS)
```

```python
import math

import jax
import jax.numpy as jnp
from jax import lax
from jax.sharding import PartitionSpec as P

SEGS = 8
NFFT = 256
F = 128
BAND = 8
LAGS = 128


epsilon = 1e-06


def forward_table():
    sample_index = jnp.arange(NFFT, dtype=jnp.int32)[:, None]
    bin_index = jnp.arange(1, F + 1, dtype=jnp.int32)[None, :]
    angles = 2.0 * jnp.pi / NFFT * (sample_index * bin_index % NFFT).astype(jnp.float32)
    norm_scale = 1.0 / math.sqrt(NFFT)
    return jnp.concatenate([jnp.cos(angles), -jnp.sin(angles)], axis=1) * norm_scale


def lag_kernel(window_total):
    bin_index = jnp.arange(1, F + 1, dtype=jnp.int32)[:, None]
    lag_shift = jnp.arange(LAGS, dtype=jnp.int32)[None, :] - LAGS // 2
    angles = 2.0 * jnp.pi / NFFT * (bin_index * lag_shift % NFFT).astype(jnp.float32)
    norm_scale = 2.0 / math.sqrt(F * SEGS * window_total)
    return jnp.stack([jnp.cos(angles) * norm_scale, -jnp.sin(angles) * norm_scale]).astype(
        jnp.bfloat16
    )


def whiten(traces, quality):
    win_count, channels = (traces.shape[0], traces.shape[1])
    segments = traces.reshape(win_count, channels, SEGS, NFFT)
    spectrum = jnp.dot(segments, forward_table(), precision=lax.Precision.HIGHEST)
    real_part = spectrum[..., :F]
    imag_part = spectrum[..., F:]
    power_sum = (real_part * real_part + imag_part * imag_part).reshape(
        win_count, channels, SEGS, F // BAND, BAND
    )
    amplitude = jnp.sqrt(jnp.mean(power_sum, axis=(2, 4)) + epsilon)
    factor = quality.astype(jnp.float32)[:, :, None] / amplitude
    factor = jnp.repeat(factor, BAND, axis=2)[:, :, None, :]
    stacked_parts = jnp.stack([real_part * factor, imag_part * factor], axis=0)
    stacked_parts = jnp.transpose(stacked_parts, (2, 0, 1, 3, 4)).reshape(
        channels, 2 * win_count * SEGS, F
    )
    return stacked_parts.astype(jnp.bfloat16)


def column_permutation(n_chan, n_win):
    per = n_chan // n_win
    return [
        (c * n_win + g, (per * g + c % per) * n_win + c // per)
        for c in range(n_chan)
        for g in range(n_win)
    ]


def body(traces, quality):
    n_chan = lax.axis_size("chan")
    n_win = lax.axis_size("win")
    per = n_chan // n_win
    kernel = lag_kernel(n_win * traces.shape[0])
    spectra = whiten(traces, quality)
    channels, parts, bins = spectra.shape
    half = parts // 2

    own = lax.all_gather(spectra, "win", axis=1, tiled=False)
    rotated = jnp.concatenate([own[:, :, half:], -own[:, :, :half]], axis=2)
    stacked = jnp.concatenate([own, rotated], axis=0).reshape(2 * channels, n_win * parts, bins)

    piece = lax.ppermute(spectra, ("chan", "win"), column_permutation(n_chan, n_win))
    theirs = lax.all_gather(piece, "chan", axis=0, tiled=False)
    theirs = theirs.reshape(n_win, per, channels, parts, bins)
    theirs = jnp.transpose(theirs, (1, 2, 0, 3, 4)).reshape(per * channels, n_win * parts, bins)

    cross = jnp.einsum(
        "iak,jak->ijk", stacked, theirs, preferred_element_type=jnp.float32
    ).astype(jnp.bfloat16)
    cross = cross.reshape(2, channels, cross.shape[1], bins)
    lags = jnp.einsum("pijk,pkt->ijt", cross, kernel, preferred_element_type=jnp.float32)
    return lags.astype(jnp.bfloat16)


def solution(mesh):
    in_specs = (P("win", "chan", None), P("win", "chan"))
    out_specs = P("chan", "win", None)
    return jax.shard_map(body, mesh=mesh, in_specs=in_specs, out_specs=out_specs, check_vma=False)
```

```python
import math

import jax
import jax.numpy as jnp
from jax import lax
from jax.sharding import PartitionSpec as P

SEGS = 8
NFFT = 256
F = 128
BAND = 8
LAGS = 128


epsilon = 1e-06


def forward_table():
    sample_index = jnp.arange(NFFT, dtype=jnp.int32)[:, None]
    bin_index = jnp.arange(1, F + 1, dtype=jnp.int32)[None, :]
    angles = 2.0 * jnp.pi / NFFT * (sample_index * bin_index % NFFT).astype(jnp.float32)
    norm_scale = 1.0 / math.sqrt(NFFT)
    return jnp.concatenate([jnp.cos(angles), -jnp.sin(angles)], axis=1) * norm_scale


def lag_kernel(window_total):
    bin_index = jnp.arange(1, F + 1, dtype=jnp.int32)[:, None]
    lag_shift = jnp.arange(LAGS, dtype=jnp.int32)[None, :] - LAGS // 2
    angles = 2.0 * jnp.pi / NFFT * (bin_index * lag_shift % NFFT).astype(jnp.float32)
    norm_scale = 2.0 / math.sqrt(F * SEGS * window_total)
    return jnp.stack([jnp.cos(angles) * norm_scale, -jnp.sin(angles) * norm_scale]).astype(
        jnp.bfloat16
    )


def whiten(traces, quality):
    win_count, channels = (traces.shape[0], traces.shape[1])
    segments = traces.reshape(win_count, channels, SEGS, NFFT)
    spectrum = jnp.dot(segments, forward_table(), precision=lax.Precision.HIGHEST)
    real_part = spectrum[..., :F]
    imag_part = spectrum[..., F:]
    power_sum = (real_part * real_part + imag_part * imag_part).reshape(
        win_count, channels, SEGS, F // BAND, BAND
    )
    amplitude = jnp.sqrt(jnp.mean(power_sum, axis=(2, 4)) + epsilon)
    factor = quality.astype(jnp.float32)[:, :, None] / amplitude
    factor = jnp.repeat(factor, BAND, axis=2)[:, :, None, :]
    stacked_parts = jnp.stack([real_part * factor, imag_part * factor], axis=0)
    stacked_parts = jnp.transpose(stacked_parts, (2, 0, 1, 3, 4)).reshape(
        channels, 2 * win_count * SEGS, F
    )
    return stacked_parts.astype(jnp.bfloat16)


def column_permutation(n_chan, n_win):
    per = n_chan // n_win
    return [
        (c * n_win + g, (per * g + c % per) * n_win + c // per)
        for c in range(n_chan)
        for g in range(n_win)
    ]


CHUNKS = 4


def body(traces, quality):
    n_chan = lax.axis_size("chan")
    n_win = lax.axis_size("win")
    per = n_chan // n_win
    kernel = lag_kernel(n_win * traces.shape[0])
    spectra = whiten(traces, quality)
    channels, parts, bins = spectra.shape
    half = parts // 2

    piece = lax.ppermute(spectra, ("chan", "win"), column_permutation(n_chan, n_win))

    received = [spectra] + [
        lax.ppermute(spectra, "win", [(s, (s + shift) % n_win) for s in range(n_win)])
        for shift in range(1, n_win)
    ]
    mirrored = [received[(-m) % n_win] for m in range(n_win)]
    doubled = jnp.stack(mirrored + mirrored, axis=1)
    own = lax.dynamic_slice_in_dim(doubled, n_win - lax.axis_index("win"), n_win, axis=1)
    rotated = jnp.concatenate([own[:, :, half:], -own[:, :, :half]], axis=2)
    stacked = jnp.concatenate([own, rotated], axis=0).reshape(2 * channels, n_win * parts, bins)

    size = channels // CHUNKS
    outs = []
    for q in range(CHUNKS):
        theirs = lax.all_gather(piece[q * size:(q + 1) * size], "chan", axis=0, tiled=False)
        theirs = theirs.reshape(n_win, per, size, parts, bins)
        theirs = jnp.transpose(theirs, (1, 2, 0, 3, 4)).reshape(per * size, n_win * parts, bins)
        cross = jnp.einsum(
            "iak,jak->ijk", stacked, theirs, preferred_element_type=jnp.float32
        ).astype(jnp.bfloat16)
        cross = cross.reshape(2, channels, per * size, bins)
        lags = jnp.einsum("pijk,pkt->ijt", cross, kernel, preferred_element_type=jnp.float32)
        outs.append(lags.astype(jnp.bfloat16).reshape(channels, per, size, LAGS))
    return jnp.stack(outs, axis=2).reshape(channels, per * channels, LAGS)


def solution(mesh):
    in_specs = (P("win", "chan", None), P("win", "chan"))
    out_specs = P("chan", "win", None)
    return jax.shard_map(body, mesh=mesh, in_specs=in_specs, out_specs=out_specs, check_vma=False)
```

```python
import math

import jax
import jax.numpy as jnp
from jax import lax
from jax.sharding import PartitionSpec as P

SEGS = 8
NFFT = 256
F = 128
BAND = 8
LAGS = 128


epsilon = 1e-06


def forward_table():
    sample_index = jnp.arange(NFFT, dtype=jnp.int32)[:, None]
    bin_index = jnp.arange(1, F + 1, dtype=jnp.int32)[None, :]
    angles = 2.0 * jnp.pi / NFFT * (sample_index * bin_index % NFFT).astype(jnp.float32)
    norm_scale = 1.0 / math.sqrt(NFFT)
    return jnp.concatenate([jnp.cos(angles), -jnp.sin(angles)], axis=1) * norm_scale


def lag_kernel(window_total):
    bin_index = jnp.arange(1, F + 1, dtype=jnp.int32)[:, None]
    lag_shift = jnp.arange(LAGS, dtype=jnp.int32)[None, :] - LAGS // 2
    angles = 2.0 * jnp.pi / NFFT * (bin_index * lag_shift % NFFT).astype(jnp.float32)
    norm_scale = 2.0 / math.sqrt(F * SEGS * window_total)
    return jnp.stack([jnp.cos(angles) * norm_scale, -jnp.sin(angles) * norm_scale]).astype(
        jnp.bfloat16
    )


def whiten(traces, quality):
    win_count, channels = (traces.shape[0], traces.shape[1])
    segments = traces.reshape(win_count, channels, SEGS, NFFT)
    spectrum = jnp.dot(segments, forward_table(), precision=lax.Precision.HIGHEST)
    real_part = spectrum[..., :F]
    imag_part = spectrum[..., F:]
    power_sum = (real_part * real_part + imag_part * imag_part).reshape(
        win_count, channels, SEGS, F // BAND, BAND
    )
    amplitude = jnp.sqrt(jnp.mean(power_sum, axis=(2, 4)) + epsilon)
    factor = quality.astype(jnp.float32)[:, :, None] / amplitude
    factor = jnp.repeat(factor, BAND, axis=2)[:, :, None, :]
    stacked_parts = jnp.stack([real_part * factor, imag_part * factor], axis=0)
    stacked_parts = jnp.transpose(stacked_parts, (2, 0, 1, 3, 4)).reshape(
        channels, 2 * win_count * SEGS, F
    )
    return stacked_parts.astype(jnp.bfloat16)


def column_permutation(n_chan, n_win):
    per = n_chan // n_win
    return [
        (c * n_win + g, (per * g + c % per) * n_win + c // per)
        for c in range(n_chan)
        for g in range(n_win)
    ]


CHUNKS = 1


def body(traces, quality):
    n_chan = lax.axis_size("chan")
    n_win = lax.axis_size("win")
    per = n_chan // n_win
    kernel = lag_kernel(n_win * traces.shape[0])
    spectra = whiten(traces, quality)
    channels, parts, bins = spectra.shape
    half = parts // 2

    piece = lax.ppermute(spectra, ("chan", "win"), column_permutation(n_chan, n_win))

    received = [spectra] + [
        lax.ppermute(spectra, "win", [(s, (s + shift) % n_win) for s in range(n_win)])
        for shift in range(1, n_win)
    ]
    mirrored = [received[(-m) % n_win] for m in range(n_win)]
    doubled = jnp.stack(mirrored + mirrored, axis=1)
    own = lax.dynamic_slice_in_dim(doubled, n_win - lax.axis_index("win"), n_win, axis=1)
    rotated = jnp.concatenate([own[:, :, half:], -own[:, :, :half]], axis=2)
    stacked = jnp.concatenate([own, rotated], axis=0).reshape(2 * channels, n_win * parts, bins)

    size = channels // CHUNKS
    outs = []
    for q in range(CHUNKS):
        theirs = lax.all_gather(piece[q * size:(q + 1) * size], "chan", axis=0, tiled=False)
        theirs = theirs.reshape(n_win, per, size, parts, bins)
        theirs = jnp.transpose(theirs, (1, 2, 0, 3, 4)).reshape(per * size, n_win * parts, bins)
        cross = jnp.einsum(
            "iak,jak->ijk", stacked, theirs, preferred_element_type=jnp.float32
        ).astype(jnp.bfloat16)
        cross = cross.reshape(2, channels, per * size, bins)
        lags = jnp.einsum("pijk,pkt->ijt", cross, kernel, preferred_element_type=jnp.float32)
        outs.append(lags.astype(jnp.bfloat16).reshape(channels, per, size, LAGS))
    return jnp.stack(outs, axis=2).reshape(channels, per * channels, LAGS)


def solution(mesh):
    in_specs = (P("win", "chan", None), P("win", "chan"))
    out_specs = P("chan", "win", None)
    return jax.shard_map(body, mesh=mesh, in_specs=in_specs, out_specs=out_specs, check_vma=False)
```

```python
import math

import jax
import jax.numpy as jnp
from jax import lax
from jax.sharding import PartitionSpec as P

SEGS = 8
NFFT = 256
F = 128
BAND = 8
LAGS = 128


epsilon = 1e-06


def forward_table():
    sample_index = jnp.arange(NFFT, dtype=jnp.int32)[:, None]
    bin_index = jnp.arange(1, F + 1, dtype=jnp.int32)[None, :]
    angles = 2.0 * jnp.pi / NFFT * (sample_index * bin_index % NFFT).astype(jnp.float32)
    norm_scale = 1.0 / math.sqrt(NFFT)
    return jnp.concatenate([jnp.cos(angles), -jnp.sin(angles)], axis=1) * norm_scale


def lag_kernel(window_total):
    bin_index = jnp.arange(1, F + 1, dtype=jnp.int32)[:, None]
    lag_shift = jnp.arange(LAGS, dtype=jnp.int32)[None, :] - LAGS // 2
    angles = 2.0 * jnp.pi / NFFT * (bin_index * lag_shift % NFFT).astype(jnp.float32)
    norm_scale = 2.0 / math.sqrt(F * SEGS * window_total)
    return jnp.stack([jnp.cos(angles) * norm_scale, -jnp.sin(angles) * norm_scale]).astype(
        jnp.bfloat16
    )


def whiten(traces, quality):
    win_count, channels = (traces.shape[0], traces.shape[1])
    segments = traces.reshape(win_count, channels, SEGS, NFFT)
    spectrum = jnp.dot(segments, forward_table(), precision=lax.Precision.HIGHEST)
    real_part = spectrum[..., :F]
    imag_part = spectrum[..., F:]
    power_sum = (real_part * real_part + imag_part * imag_part).reshape(
        win_count, channels, SEGS, F // BAND, BAND
    )
    amplitude = jnp.sqrt(jnp.mean(power_sum, axis=(2, 4)) + epsilon)
    factor = quality.astype(jnp.float32)[:, :, None] / amplitude
    factor = jnp.repeat(factor, BAND, axis=2)[:, :, None, :]
    stacked_parts = jnp.stack([real_part * factor, imag_part * factor], axis=0)
    stacked_parts = jnp.transpose(stacked_parts, (2, 0, 1, 3, 4)).reshape(
        channels, 2 * win_count * SEGS, F
    )
    return stacked_parts.astype(jnp.bfloat16)


def column_permutation(n_chan, n_win):
    per = n_chan // n_win
    return [
        (c * n_win + g, (per * g + c % per) * n_win + c // per)
        for c in range(n_chan)
        for g in range(n_win)
    ]


CHAN_AXES = (("z", 8), ("yh", 2), ("x", 4))
STREAMS = ((19, ("yh", "z", "x")), (13, ("yh", "x", "z")))
ALL_AXES = tuple(name for name, _ in CHAN_AXES) + ("win",)


def ring_all_gather(unit, axis, n):
    me = lax.axis_index(axis)
    blocks = [(0, unit)]
    if n == 2:
        blocks.append((1, lax.ppermute(unit, axis, [(0, 1), (1, 0)])))
    elif n > 2:
        up = [(i, (i + 1) % n) for i in range(n)]
        down = [(i, (i - 1) % n) for i in range(n)]
        forward = backward = unit
        for step in range(1, n // 2 + 1):
            if 2 * step < n:
                forward = lax.ppermute(forward, axis, up)
                backward = lax.ppermute(backward, axis, down)
                blocks += [(-step, forward), (step, backward)]
            else:
                half = unit.shape[-2] // 2
                first = lax.ppermute(forward[..., :half, :], axis, up)
                second = lax.ppermute(backward[..., half:, :], axis, down)
                blocks.append((step, jnp.concatenate([first, second], axis=-2)))
    buffer = jnp.zeros((n,) + unit.shape, unit.dtype)
    for offset, block in blocks:
        buffer = lax.dynamic_update_index_in_dim(buffer, block, (me + offset % n) % n, 0)
    return buffer


def gather_chan(unit, order):
    sizes = dict(CHAN_AXES)
    for axis in order:
        unit = ring_all_gather(unit, axis, sizes[axis])
    stages = list(reversed(order))
    perm = [stages.index(name) for name, _ in CHAN_AXES]
    return jnp.transpose(unit, perm + list(range(len(order), unit.ndim)))


def body(traces, quality):
    n_win = lax.axis_size("win")
    n_chan = 1
    for name, size in CHAN_AXES:
        n_chan *= size
    per = n_chan // n_win
    kernel = lag_kernel(n_win * traces.shape[0])
    spectra = whiten(traces, quality)
    channels, parts, bins = spectra.shape
    half = parts // 2

    piece = lax.ppermute(spectra, ALL_AXES, column_permutation(n_chan, n_win))

    received = [spectra] + [
        lax.ppermute(spectra, "win", [(s, (s + shift) % n_win) for s in range(n_win)])
        for shift in range(1, n_win)
    ]
    mirrored = [received[(-m) % n_win] for m in range(n_win)]
    doubled = jnp.stack(mirrored + mirrored, axis=1)
    own = lax.dynamic_slice_in_dim(doubled, n_win - lax.axis_index("win"), n_win, axis=1)
    rotated = jnp.concatenate([own[:, :, half:], -own[:, :, :half]], axis=2)
    stacked = jnp.concatenate([own, rotated], axis=0).reshape(2 * channels, n_win * parts, bins)

    outs = []
    first = 0
    for size, order in STREAMS:
        theirs = gather_chan(piece[first:first + size], order)
        first += size
        theirs = theirs.reshape(n_win, per, size, parts, bins)
        theirs = jnp.transpose(theirs, (1, 2, 0, 3, 4)).reshape(per * size, n_win * parts, bins)
        cross = jnp.einsum(
            "iak,jak->ijk", stacked, theirs, preferred_element_type=jnp.float32
        ).astype(jnp.bfloat16)
        cross = cross.reshape(2, channels, per * size, bins)
        lags = jnp.einsum("pijk,pkt->ijt", cross, kernel, preferred_element_type=jnp.float32)
        outs.append(lags.astype(jnp.bfloat16).reshape(channels, per, size, LAGS))
    return jnp.concatenate(outs, axis=2).reshape(channels, per * channels, LAGS)


def solution(mesh):
    names = tuple(name for name, _ in CHAN_AXES)
    shape = tuple(size for _, size in CHAN_AXES) + (mesh.shape["win"],)
    fine = jax.sharding.Mesh(mesh.devices.reshape(shape), ALL_AXES)
    in_specs = (P("win", names, None), P("win", names))
    out_specs = P(names, "win", None)
    return jax.shard_map(body, mesh=fine, in_specs=in_specs, out_specs=out_specs, check_vma=False)
```

```python
import math

import jax
import jax.numpy as jnp
from jax import lax
from jax.sharding import PartitionSpec as P

SEGS = 8
NFFT = 256
F = 128
BAND = 8
LAGS = 128


epsilon = 1e-06


def forward_table():
    sample_index = jnp.arange(NFFT, dtype=jnp.int32)[:, None]
    bin_index = jnp.arange(1, F + 1, dtype=jnp.int32)[None, :]
    angles = 2.0 * jnp.pi / NFFT * (sample_index * bin_index % NFFT).astype(jnp.float32)
    norm_scale = 1.0 / math.sqrt(NFFT)
    return jnp.concatenate([jnp.cos(angles), -jnp.sin(angles)], axis=1) * norm_scale


def lag_kernel(window_total):
    bin_index = jnp.arange(1, F + 1, dtype=jnp.int32)[:, None]
    lag_shift = jnp.arange(LAGS, dtype=jnp.int32)[None, :] - LAGS // 2
    angles = 2.0 * jnp.pi / NFFT * (bin_index * lag_shift % NFFT).astype(jnp.float32)
    norm_scale = 2.0 / math.sqrt(F * SEGS * window_total)
    return jnp.stack([jnp.cos(angles) * norm_scale, -jnp.sin(angles) * norm_scale]).astype(
        jnp.bfloat16
    )


def whiten(traces, quality):
    win_count, channels = (traces.shape[0], traces.shape[1])
    segments = traces.reshape(win_count, channels, SEGS, NFFT)
    spectrum = jnp.dot(segments, forward_table(), precision=lax.Precision.HIGHEST)
    real_part = spectrum[..., :F]
    imag_part = spectrum[..., F:]
    power_sum = (real_part * real_part + imag_part * imag_part).reshape(
        win_count, channels, SEGS, F // BAND, BAND
    )
    amplitude = jnp.sqrt(jnp.mean(power_sum, axis=(2, 4)) + epsilon)
    factor = quality.astype(jnp.float32)[:, :, None] / amplitude
    factor = jnp.repeat(factor, BAND, axis=2)[:, :, None, :]
    stacked_parts = jnp.stack([real_part * factor, imag_part * factor], axis=0)
    stacked_parts = jnp.transpose(stacked_parts, (2, 0, 1, 3, 4)).reshape(
        channels, 2 * win_count * SEGS, F
    )
    return stacked_parts.astype(jnp.bfloat16)


def column_permutation(n_chan, n_win):
    per = n_chan // n_win
    return [
        (c * n_win + g, (per * g + c % per) * n_win + c // per)
        for c in range(n_chan)
        for g in range(n_win)
    ]


CHAN_AXES = (("z", 8), ("yh", 2), ("x", 4))
STREAMS = ((19, ("yh", "z", "x")), (13, (("yh", "x"), "z")))
ALL_AXES = tuple(name for name, _ in CHAN_AXES) + ("win",)


def ring_all_gather(unit, axis, n):
    me = lax.axis_index(axis)
    blocks = [(0, unit)]
    if n == 2:
        blocks.append((1, lax.ppermute(unit, axis, [(0, 1), (1, 0)])))
    elif n > 2:
        up = [(i, (i + 1) % n) for i in range(n)]
        down = [(i, (i - 1) % n) for i in range(n)]
        forward = backward = unit
        for step in range(1, n // 2 + 1):
            if 2 * step < n:
                forward = lax.ppermute(forward, axis, up)
                backward = lax.ppermute(backward, axis, down)
                blocks += [(-step, forward), (step, backward)]
            else:
                half = unit.shape[-2] // 2
                first = lax.ppermute(forward[..., :half, :], axis, up)
                second = lax.ppermute(backward[..., half:, :], axis, down)
                blocks.append((step, jnp.concatenate([first, second], axis=-2)))
    buffer = jnp.zeros((n,) + unit.shape, unit.dtype)
    for offset, block in blocks:
        buffer = lax.dynamic_update_index_in_dim(buffer, block, (me + offset % n) % n, 0)
    return buffer


def gather_chan(unit, order):
    sizes = dict(CHAN_AXES)
    stages = []
    for stage in order:
        if isinstance(stage, tuple):
            count = 1
            for axis in stage:
                count *= sizes[axis]
            unit = lax.all_gather(unit, stage, axis=0, tiled=False)
            unit = unit.reshape(tuple(sizes[axis] for axis in stage) + unit.shape[1:])
            stages = list(stage) + stages
        else:
            unit = ring_all_gather(unit, stage, sizes[stage])
            stages = [stage] + stages
    perm = [stages.index(name) for name, _ in CHAN_AXES]
    return jnp.transpose(unit, perm + list(range(len(stages), unit.ndim)))


def body(traces, quality):
    n_win = lax.axis_size("win")
    n_chan = 1
    for name, size in CHAN_AXES:
        n_chan *= size
    per = n_chan // n_win
    kernel = lag_kernel(n_win * traces.shape[0])
    spectra = whiten(traces, quality)
    channels, parts, bins = spectra.shape
    half = parts // 2

    piece = lax.ppermute(spectra, ALL_AXES, column_permutation(n_chan, n_win))

    own = lax.all_gather(spectra, "win", axis=1, tiled=False)
    rotated = jnp.concatenate([own[:, :, half:], -own[:, :, :half]], axis=2)
    stacked = jnp.concatenate([own, rotated], axis=0).reshape(2 * channels, n_win * parts, bins)

    outs = []
    first = 0
    for size, order in STREAMS:
        theirs = gather_chan(piece[first:first + size], order)
        first += size
        theirs = theirs.reshape(n_win, per, size, parts, bins)
        theirs = jnp.transpose(theirs, (1, 2, 0, 3, 4)).reshape(per * size, n_win * parts, bins)
        cross = jnp.einsum(
            "iak,jak->ijk", stacked, theirs, preferred_element_type=jnp.float32
        ).astype(jnp.bfloat16)
        cross = cross.reshape(2, channels, per * size, bins)
        lags = jnp.einsum("pijk,pkt->ijt", cross, kernel, preferred_element_type=jnp.float32)
        outs.append(lags.astype(jnp.bfloat16).reshape(channels, per, size, LAGS))
    return jnp.concatenate(outs, axis=2).reshape(channels, per * channels, LAGS)


def solution(mesh):
    names = tuple(name for name, _ in CHAN_AXES)
    shape = tuple(size for _, size in CHAN_AXES) + (mesh.shape["win"],)
    fine = jax.sharding.Mesh(mesh.devices.reshape(shape), ALL_AXES)
    in_specs = (P("win", names, None), P("win", names))
    out_specs = P(names, "win", None)
    return jax.shard_map(body, mesh=fine, in_specs=in_specs, out_specs=out_specs, check_vma=False)
```

```python
import math

import jax
import jax.numpy as jnp
from jax import lax
from jax.sharding import PartitionSpec as P

SEGS = 8
NFFT = 256
F = 128
BAND = 8
LAGS = 128


epsilon = 1e-06


def forward_table():
    sample_index = jnp.arange(NFFT, dtype=jnp.int32)[:, None]
    bin_index = jnp.arange(1, F + 1, dtype=jnp.int32)[None, :]
    angles = 2.0 * jnp.pi / NFFT * (sample_index * bin_index % NFFT).astype(jnp.float32)
    norm_scale = 1.0 / math.sqrt(NFFT)
    return jnp.concatenate([jnp.cos(angles), -jnp.sin(angles)], axis=1) * norm_scale


def lag_kernel(window_total):
    bin_index = jnp.arange(1, F + 1, dtype=jnp.int32)[:, None]
    lag_shift = jnp.arange(LAGS, dtype=jnp.int32)[None, :] - LAGS // 2
    angles = 2.0 * jnp.pi / NFFT * (bin_index * lag_shift % NFFT).astype(jnp.float32)
    norm_scale = 2.0 / math.sqrt(F * SEGS * window_total)
    return jnp.stack([jnp.cos(angles) * norm_scale, -jnp.sin(angles) * norm_scale]).astype(
        jnp.bfloat16
    )


def whiten(traces, quality):
    win_count, channels = (traces.shape[0], traces.shape[1])
    segments = traces.reshape(win_count, channels, SEGS, NFFT)
    spectrum = jnp.dot(segments, forward_table(), precision=lax.Precision.HIGHEST)
    real_part = spectrum[..., :F]
    imag_part = spectrum[..., F:]
    power_sum = (real_part * real_part + imag_part * imag_part).reshape(
        win_count, channels, SEGS, F // BAND, BAND
    )
    amplitude = jnp.sqrt(jnp.mean(power_sum, axis=(2, 4)) + epsilon)
    factor = quality.astype(jnp.float32)[:, :, None] / amplitude
    factor = jnp.repeat(factor, BAND, axis=2)[:, :, None, :]
    stacked_parts = jnp.stack([real_part * factor, imag_part * factor], axis=0)
    stacked_parts = jnp.transpose(stacked_parts, (2, 0, 1, 3, 4)).reshape(
        channels, 2 * win_count * SEGS, F
    )
    return stacked_parts.astype(jnp.bfloat16)


def column_permutation(n_chan, n_win):
    per = n_chan // n_win
    return [
        (c * n_win + g, (per * g + c % per) * n_win + c // per)
        for c in range(n_chan)
        for g in range(n_win)
    ]


CHAN_AXES = (("z", 8), ("yh", 2), ("x", 4))
STREAMS = ((19, ("z", "x")), (13, ("x", "z")))
ALL_AXES = tuple(name for name, _ in CHAN_AXES) + ("win",)


def ring_all_gather(unit, axis, n, relative=False):
    me = lax.axis_index(axis)
    blocks = [(0, unit)]
    if n == 2:
        blocks.append((1, lax.ppermute(unit, axis, [(0, 1), (1, 0)])))
    elif n > 2:
        up = [(i, (i + 1) % n) for i in range(n)]
        down = [(i, (i - 1) % n) for i in range(n)]
        forward = backward = unit
        for step in range(1, n // 2 + 1):
            if 2 * step < n:
                forward = lax.ppermute(forward, axis, up)
                backward = lax.ppermute(backward, axis, down)
                blocks += [(-step, forward), (step, backward)]
            else:
                half = unit.shape[-2] // 2
                first = lax.ppermute(forward[..., :half, :], axis, up)
                second = lax.ppermute(backward[..., half:, :], axis, down)
                blocks.append((step, jnp.concatenate([first, second], axis=-2)))
    if relative:
        ordered = dict((offset % n, block) for offset, block in blocks)
        return jnp.stack([ordered[d] for d in range(n)])
    buffer = jnp.zeros((n,) + unit.shape, unit.dtype)
    for offset, block in blocks:
        buffer = lax.dynamic_update_index_in_dim(buffer, block, (me + offset % n) % n, 0)
    return buffer


def gather_chan(unit, order, done):
    sizes = dict(CHAN_AXES)
    stages = list(done)
    for number, axis in enumerate(order):
        unit = ring_all_gather(unit, axis, sizes[axis], relative=number == len(order) - 1 and axis == "x")
        stages = [axis] + stages
    perm = [stages.index(name) for name, _ in CHAN_AXES]
    return jnp.transpose(unit, perm + list(range(len(stages), unit.ndim)))


def roll_axis(array, axis, shift):
    n = array.shape[axis]
    doubled = jnp.concatenate([array, array], axis=axis)
    return lax.dynamic_slice_in_dim(doubled, n - shift, n, axis=axis)


def body(traces, quality):
    n_win = lax.axis_size("win")
    n_chan = 1
    for name, size in CHAN_AXES:
        n_chan *= size
    per = n_chan // n_win
    kernel = lag_kernel(n_win * traces.shape[0])
    spectra = whiten(traces, quality)
    channels, parts, bins = spectra.shape
    half = parts // 2

    piece = lax.ppermute(spectra, ALL_AXES, column_permutation(n_chan, n_win))

    own = lax.all_gather(spectra, "win", axis=1, tiled=False)
    rotated = jnp.concatenate([own[:, :, half:], -own[:, :, :half]], axis=2)
    stacked = jnp.concatenate([own, rotated], axis=0).reshape(2 * channels, n_win * parts, bins)

    sizes = dict(CHAN_AXES)
    shared = ring_all_gather(piece, "yh", sizes["yh"])
    outs = []
    first = 0
    for size, order in STREAMS:
        theirs = gather_chan(shared[:, first:first + size], order, ["yh"])
        first += size
        theirs = theirs.reshape(n_win, per, size, parts, bins)
        theirs = jnp.transpose(theirs, (1, 2, 0, 3, 4)).reshape(per * size, n_win * parts, bins)
        cross = jnp.einsum(
            "iak,jak->ijk", stacked, theirs, preferred_element_type=jnp.float32
        ).astype(jnp.bfloat16)
        cross = cross.reshape(2, channels, per * size, bins)
        lags = jnp.einsum("pijk,pkt->ijt", cross, kernel, preferred_element_type=jnp.float32)
        lags = lags.astype(jnp.bfloat16).reshape(
            (channels, per // (sizes["yh"] * sizes["x"]), sizes["yh"], sizes["x"], size, LAGS)
        )
        if order[-1] == "x":
            lags = roll_axis(lags, 3, lax.axis_index("x"))
        outs.append(lags.reshape(channels, per, size, LAGS))
    return jnp.concatenate(outs, axis=2).reshape(channels, per * channels, LAGS)


def solution(mesh):
    names = tuple(name for name, _ in CHAN_AXES)
    shape = tuple(size for _, size in CHAN_AXES) + (mesh.shape["win"],)
    fine = jax.sharding.Mesh(mesh.devices.reshape(shape), ALL_AXES)
    in_specs = (P("win", names, None), P("win", names))
    out_specs = P(names, "win", None)
    return jax.shard_map(body, mesh=fine, in_specs=in_specs, out_specs=out_specs, check_vma=False)
```

```python
import math

import jax
import jax.numpy as jnp
from jax import lax
from jax.sharding import PartitionSpec as P

SEGS = 8
NFFT = 256
F = 128
BAND = 8
LAGS = 128


epsilon = 1e-06


def forward_table():
    sample_index = jnp.arange(NFFT, dtype=jnp.int32)[:, None]
    bin_index = jnp.arange(1, F + 1, dtype=jnp.int32)[None, :]
    angles = 2.0 * jnp.pi / NFFT * (sample_index * bin_index % NFFT).astype(jnp.float32)
    norm_scale = 1.0 / math.sqrt(NFFT)
    return jnp.concatenate([jnp.cos(angles), -jnp.sin(angles)], axis=1) * norm_scale


def lag_kernel(window_total):
    bin_index = jnp.arange(1, F + 1, dtype=jnp.int32)[:, None]
    lag_shift = jnp.arange(LAGS, dtype=jnp.int32)[None, :] - LAGS // 2
    angles = 2.0 * jnp.pi / NFFT * (bin_index * lag_shift % NFFT).astype(jnp.float32)
    norm_scale = 2.0 / math.sqrt(F * SEGS * window_total)
    return jnp.stack([jnp.cos(angles) * norm_scale, -jnp.sin(angles) * norm_scale]).astype(
        jnp.bfloat16
    )


def whiten(traces, quality):
    win_count, channels = (traces.shape[0], traces.shape[1])
    segments = traces.reshape(win_count, channels, SEGS, NFFT)
    spectrum = jnp.dot(segments, forward_table(), precision=lax.Precision.HIGHEST)
    real_part = spectrum[..., :F]
    imag_part = spectrum[..., F:]
    power_sum = (real_part * real_part + imag_part * imag_part).reshape(
        win_count, channels, SEGS, F // BAND, BAND
    )
    amplitude = jnp.sqrt(jnp.mean(power_sum, axis=(2, 4)) + epsilon)
    factor = quality.astype(jnp.float32)[:, :, None] / amplitude
    factor = jnp.repeat(factor, BAND, axis=2)[:, :, None, :]
    stacked_parts = jnp.stack([real_part * factor, imag_part * factor], axis=0)
    stacked_parts = jnp.transpose(stacked_parts, (2, 0, 1, 3, 4)).reshape(
        channels, 2 * win_count * SEGS, F
    )
    return stacked_parts.astype(jnp.bfloat16)


def column_permutation(n_chan, n_win):
    per = n_chan // n_win
    return [
        (c * n_win + g, (per * g + c % per) * n_win + c // per)
        for c in range(n_chan)
        for g in range(n_win)
    ]


CHAN_AXES = (("z", 8), ("yh", 2), ("x", 4))
STREAMS = ((6, (("z", "yh", "x"),)), (26, ("yh", "z", "x")))
ALL_AXES = tuple(name for name, _ in CHAN_AXES) + ("win",)


def ring_all_gather(unit, axis, n):
    me = lax.axis_index(axis)
    blocks = [(0, unit)]
    if n == 2:
        blocks.append((1, lax.ppermute(unit, axis, [(0, 1), (1, 0)])))
    elif n > 2:
        up = [(i, (i + 1) % n) for i in range(n)]
        down = [(i, (i - 1) % n) for i in range(n)]
        forward = backward = unit
        for step in range(1, n // 2 + 1):
            if 2 * step < n:
                forward = lax.ppermute(forward, axis, up)
                backward = lax.ppermute(backward, axis, down)
                blocks += [(-step, forward), (step, backward)]
            else:
                half = unit.shape[-2] // 2
                first = lax.ppermute(forward[..., :half, :], axis, up)
                second = lax.ppermute(backward[..., half:, :], axis, down)
                blocks.append((step, jnp.concatenate([first, second], axis=-2)))
    buffer = jnp.zeros((n,) + unit.shape, unit.dtype)
    for offset, block in blocks:
        buffer = lax.dynamic_update_index_in_dim(buffer, block, (me + offset % n) % n, 0)
    return buffer


def gather_chan(unit, order):
    sizes = dict(CHAN_AXES)
    stages = []
    for stage in order:
        if isinstance(stage, tuple):
            unit = lax.all_gather(unit, stage, axis=0, tiled=False)
            unit = unit.reshape(tuple(sizes[axis] for axis in stage) + unit.shape[1:])
            stages = list(stage) + stages
        else:
            unit = ring_all_gather(unit, stage, sizes[stage])
            stages = [stage] + stages
    perm = [stages.index(name) for name, _ in CHAN_AXES]
    return jnp.transpose(unit, perm + list(range(len(stages), unit.ndim)))


def body(traces, quality):
    n_win = lax.axis_size("win")
    n_chan = 1
    for name, size in CHAN_AXES:
        n_chan *= size
    per = n_chan // n_win
    kernel = lag_kernel(n_win * traces.shape[0])
    spectra = whiten(traces, quality)
    channels, parts, bins = spectra.shape
    half = parts // 2

    piece = lax.ppermute(spectra, ALL_AXES, column_permutation(n_chan, n_win))

    received = [spectra] + [
        lax.ppermute(spectra, "win", [(s, (s + shift) % n_win) for s in range(n_win)])
        for shift in range(1, n_win)
    ]
    mirrored = [received[(-m) % n_win] for m in range(n_win)]
    doubled = jnp.stack(mirrored + mirrored, axis=1)
    own = lax.dynamic_slice_in_dim(doubled, n_win - lax.axis_index("win"), n_win, axis=1)
    rotated = jnp.concatenate([own[:, :, half:], -own[:, :, :half]], axis=2)
    stacked = jnp.concatenate([own, rotated], axis=0).reshape(2 * channels, n_win * parts, bins)

    outs = []
    first = 0
    for size, order in STREAMS:
        theirs = gather_chan(piece[first:first + size], order)
        first += size
        theirs = theirs.reshape(n_win, per, size, parts, bins)
        theirs = jnp.transpose(theirs, (1, 2, 0, 3, 4)).reshape(per * size, n_win * parts, bins)
        cross = jnp.einsum(
            "iak,jak->ijk", stacked, theirs, preferred_element_type=jnp.float32
        ).astype(jnp.bfloat16)
        cross = cross.reshape(2, channels, per * size, bins)
        lags = jnp.einsum("pijk,pkt->ijt", cross, kernel, preferred_element_type=jnp.float32)
        outs.append(lags.astype(jnp.bfloat16).reshape(channels, per, size, LAGS))
    return jnp.concatenate(outs, axis=2).reshape(channels, per * channels, LAGS)


def solution(mesh):
    names = tuple(name for name, _ in CHAN_AXES)
    shape = tuple(size for _, size in CHAN_AXES) + (mesh.shape["win"],)
    fine = jax.sharding.Mesh(mesh.devices.reshape(shape), ALL_AXES)
    in_specs = (P("win", names, None), P("win", names))
    out_specs = P(names, "win", None)
    return jax.shard_map(body, mesh=fine, in_specs=in_specs, out_specs=out_specs, check_vma=False)
```

```python
import math

import jax
import jax.numpy as jnp
from jax import lax
from jax.sharding import PartitionSpec as P

SEGS = 8
NFFT = 256
F = 128
BAND = 8
LAGS = 128


epsilon = 1e-06


def forward_table():
    sample_index = jnp.arange(NFFT, dtype=jnp.int32)[:, None]
    bin_index = jnp.arange(1, F + 1, dtype=jnp.int32)[None, :]
    angles = 2.0 * jnp.pi / NFFT * (sample_index * bin_index % NFFT).astype(jnp.float32)
    norm_scale = 1.0 / math.sqrt(NFFT)
    return jnp.concatenate([jnp.cos(angles), -jnp.sin(angles)], axis=1) * norm_scale


def lag_kernel(window_total):
    bin_index = jnp.arange(1, F + 1, dtype=jnp.int32)[:, None]
    lag_shift = jnp.arange(LAGS, dtype=jnp.int32)[None, :] - LAGS // 2
    angles = 2.0 * jnp.pi / NFFT * (bin_index * lag_shift % NFFT).astype(jnp.float32)
    norm_scale = 2.0 / math.sqrt(F * SEGS * window_total)
    return jnp.stack([jnp.cos(angles) * norm_scale, -jnp.sin(angles) * norm_scale]).astype(
        jnp.bfloat16
    )


def whiten(traces, quality):
    win_count, channels = (traces.shape[0], traces.shape[1])
    segments = traces.reshape(win_count, channels, SEGS, NFFT)
    spectrum = jnp.dot(segments, forward_table(), precision=lax.Precision.HIGHEST)
    real_part = spectrum[..., :F]
    imag_part = spectrum[..., F:]
    power_sum = (real_part * real_part + imag_part * imag_part).reshape(
        win_count, channels, SEGS, F // BAND, BAND
    )
    amplitude = jnp.sqrt(jnp.mean(power_sum, axis=(2, 4)) + epsilon)
    factor = quality.astype(jnp.float32)[:, :, None] / amplitude
    factor = jnp.repeat(factor, BAND, axis=2)[:, :, None, :]
    stacked_parts = jnp.stack([real_part * factor, imag_part * factor], axis=0)
    stacked_parts = jnp.transpose(stacked_parts, (2, 0, 1, 3, 4)).reshape(
        channels, 2 * win_count * SEGS, F
    )
    return stacked_parts.astype(jnp.bfloat16)


def column_permutation(n_chan, n_win):
    per = n_chan // n_win
    return [
        (c * n_win + g, (per * g + c % per) * n_win + c // per)
        for c in range(n_chan)
        for g in range(n_win)
    ]


CHAN_AXES = (("z", 8), ("yh", 2), ("x", 4))
STREAMS = ((19, ("yh", "z", "x")), (13, ("yh", "x", "z")))
ALL_AXES = tuple(name for name, _ in CHAN_AXES) + ("win",)


def ring_all_gather(unit, axis, n, as_blocks=False):
    me = lax.axis_index(axis)
    blocks = [(0, unit)]
    if n == 2:
        blocks.append((1, lax.ppermute(unit, axis, [(0, 1), (1, 0)])))
    elif n > 2:
        up = [(i, (i + 1) % n) for i in range(n)]
        down = [(i, (i - 1) % n) for i in range(n)]
        forward = backward = unit
        for step in range(1, n // 2 + 1):
            if 2 * step < n:
                forward = lax.ppermute(forward, axis, up)
                backward = lax.ppermute(backward, axis, down)
                blocks += [(-step, forward), (step, backward)]
            else:
                half = unit.shape[-2] // 2
                first = lax.ppermute(forward[..., :half, :], axis, up)
                second = lax.ppermute(backward[..., half:, :], axis, down)
                blocks.append((step, jnp.concatenate([first, second], axis=-2)))
    if as_blocks:
        return blocks
    buffer = jnp.zeros((n,) + unit.shape, unit.dtype)
    for offset, block in blocks:
        buffer = lax.dynamic_update_index_in_dim(buffer, block, (me + offset % n) % n, 0)
    return buffer


def gather_chan(unit, order):
    sizes = dict(CHAN_AXES)
    for axis in order:
        unit = ring_all_gather(unit, axis, sizes[axis])
    stages = list(reversed(order))
    perm = [stages.index(name) for name, _ in CHAN_AXES]
    return jnp.transpose(unit, perm + list(range(len(order), unit.ndim)))


def body(traces, quality):
    n_win = lax.axis_size("win")
    n_chan = 1
    for name, size in CHAN_AXES:
        n_chan *= size
    per = n_chan // n_win
    kernel = lag_kernel(n_win * traces.shape[0])
    spectra = whiten(traces, quality)
    channels, parts, bins = spectra.shape
    half = parts // 2

    piece = lax.ppermute(spectra, ALL_AXES, column_permutation(n_chan, n_win))

    received = [spectra] + [
        lax.ppermute(spectra, "win", [(s, (s + shift) % n_win) for s in range(n_win)])
        for shift in range(1, n_win)
    ]
    mirrored = [received[(-m) % n_win] for m in range(n_win)]
    doubled = jnp.stack(mirrored + mirrored, axis=1)
    own = lax.dynamic_slice_in_dim(doubled, n_win - lax.axis_index("win"), n_win, axis=1)
    rotated = jnp.concatenate([own[:, :, half:], -own[:, :, :half]], axis=2)
    stacked = jnp.concatenate([own, rotated], axis=0).reshape(2 * channels, n_win * parts, bins)

    def lag_columns(theirs):
        columns = theirs.shape[1]
        theirs = jnp.transpose(theirs, (1, 0, 2, 3)).reshape(columns, n_win * parts, bins)
        cross = jnp.einsum(
            "iak,jak->ijk", stacked, theirs, preferred_element_type=jnp.float32
        ).astype(jnp.bfloat16)
        cross = cross.reshape(2, channels, columns, bins)
        lags = jnp.einsum("pijk,pkt->ijt", cross, kernel, preferred_element_type=jnp.float32)
        return lags.astype(jnp.bfloat16)

    sizes = dict(CHAN_AXES)
    n_x = sizes["x"]
    outs = []
    first = 0
    for size, order in STREAMS:
        part = piece[first:first + size]
        first += size
        if order[-1] == "x":
            unit = part
            for axis in order[:-1]:
                unit = ring_all_gather(unit, axis, sizes[axis])
            stages = list(reversed(order[:-1]))
            names = [name for name, _ in CHAN_AXES if name != "x"]
            perm = [stages.index(name) for name in names]
            unit = jnp.transpose(unit, perm + list(range(len(perm), unit.ndim)))
            result = jnp.zeros(
                (channels, per // (sizes["yh"] * n_x), sizes["yh"], n_x, size, LAGS), jnp.bfloat16
            )
            for offset, block in ring_all_gather(unit, "x", n_x, as_blocks=True):
                block = block.reshape((n_win, per // n_x) + block.shape[2:])
                lags = lag_columns(block.reshape(n_win, -1, parts, bins))
                lags = lags.reshape(channels, per // (sizes["yh"] * n_x), sizes["yh"], 1, size, LAGS)
                place = (lax.axis_index("x") + offset % n_x) % n_x
                result = lax.dynamic_update_index_in_dim(result, lags, place, 3)
            outs.append(result.reshape(channels, per, size, LAGS))
        else:
            theirs = gather_chan(part, order)
            theirs = theirs.reshape(n_win, per * size, parts, bins)
            outs.append(lag_columns(theirs).reshape(channels, per, size, LAGS))
    return jnp.concatenate(outs, axis=2).reshape(channels, per * channels, LAGS)


def solution(mesh):
    names = tuple(name for name, _ in CHAN_AXES)
    shape = tuple(size for _, size in CHAN_AXES) + (mesh.shape["win"],)
    fine = jax.sharding.Mesh(mesh.devices.reshape(shape), ALL_AXES)
    in_specs = (P("win", names, None), P("win", names))
    out_specs = P(names, "win", None)
    return jax.shard_map(body, mesh=fine, in_specs=in_specs, out_specs=out_specs, check_vma=False)
```

```python
import math

import jax
import jax.numpy as jnp
from jax import lax
from jax.sharding import PartitionSpec as P

SEGS = 8
NFFT = 256
F = 128
BAND = 8
LAGS = 128


epsilon = 1e-06


def forward_table():
    sample_index = jnp.arange(NFFT, dtype=jnp.int32)[:, None]
    bin_index = jnp.arange(1, F + 1, dtype=jnp.int32)[None, :]
    angles = 2.0 * jnp.pi / NFFT * (sample_index * bin_index % NFFT).astype(jnp.float32)
    norm_scale = 1.0 / math.sqrt(NFFT)
    return jnp.concatenate([jnp.cos(angles), -jnp.sin(angles)], axis=1) * norm_scale


def lag_kernel(window_total):
    bin_index = jnp.arange(1, F + 1, dtype=jnp.int32)[:, None]
    lag_shift = jnp.arange(LAGS, dtype=jnp.int32)[None, :] - LAGS // 2
    angles = 2.0 * jnp.pi / NFFT * (bin_index * lag_shift % NFFT).astype(jnp.float32)
    norm_scale = 2.0 / math.sqrt(F * SEGS * window_total)
    return jnp.stack([jnp.cos(angles) * norm_scale, -jnp.sin(angles) * norm_scale]).astype(
        jnp.bfloat16
    )


def whiten(traces, quality):
    win_count, channels = (traces.shape[0], traces.shape[1])
    segments = traces.reshape(win_count, channels, SEGS, NFFT)
    spectrum = jnp.dot(segments, forward_table(), precision=lax.Precision.HIGHEST)
    real_part = spectrum[..., :F]
    imag_part = spectrum[..., F:]
    power_sum = (real_part * real_part + imag_part * imag_part).reshape(
        win_count, channels, SEGS, F // BAND, BAND
    )
    amplitude = jnp.sqrt(jnp.mean(power_sum, axis=(2, 4)) + epsilon)
    factor = quality.astype(jnp.float32)[:, :, None] / amplitude
    factor = jnp.repeat(factor, BAND, axis=2)[:, :, None, :]
    stacked_parts = jnp.stack([real_part * factor, imag_part * factor], axis=0)
    stacked_parts = jnp.transpose(stacked_parts, (2, 0, 1, 3, 4)).reshape(
        channels, 2 * win_count * SEGS, F
    )
    return stacked_parts.astype(jnp.bfloat16)


def column_permutation(n_chan, n_win):
    per = n_chan // n_win
    return [
        (c * n_win + g, (per * g + c % per) * n_win + c // per)
        for c in range(n_chan)
        for g in range(n_win)
    ]


CHAN_AXES = (("z", 8), ("yh", 2), ("x", 4))
STREAMS = ((16, ("yh", "z", "x")), (16, ("yh", "x", "z")))
ALL_AXES = tuple(name for name, _ in CHAN_AXES) + ("win",)


def ring_all_gather(unit, axis, n):
    me = lax.axis_index(axis)
    blocks = [(0, unit)]
    if n == 2:
        blocks.append((1, lax.ppermute(unit, axis, [(0, 1), (1, 0)])))
    elif n > 2:
        up = [(i, (i + 1) % n) for i in range(n)]
        down = [(i, (i - 1) % n) for i in range(n)]
        forward = backward = unit
        for step in range(1, n // 2 + 1):
            if 2 * step < n:
                forward = lax.ppermute(forward, axis, up)
                backward = lax.ppermute(backward, axis, down)
                blocks += [(-step, forward), (step, backward)]
            else:
                half = unit.shape[-2] // 2
                first = lax.ppermute(forward[..., :half, :], axis, up)
                second = lax.ppermute(backward[..., half:, :], axis, down)
                blocks.append((step, jnp.concatenate([first, second], axis=-2)))
    buffer = jnp.zeros((n,) + unit.shape, unit.dtype)
    for offset, block in blocks:
        buffer = lax.dynamic_update_index_in_dim(buffer, block, (me + offset % n) % n, 0)
    return buffer


def gather_chan(unit, order):
    sizes = dict(CHAN_AXES)
    for axis in order:
        unit = ring_all_gather(unit, axis, sizes[axis])
    stages = list(reversed(order))
    perm = [stages.index(name) for name, _ in CHAN_AXES]
    return jnp.transpose(unit, perm + list(range(len(order), unit.ndim)))


def body(traces, quality):
    n_win = lax.axis_size("win")
    n_chan = 1
    for name, size in CHAN_AXES:
        n_chan *= size
    per = n_chan // n_win
    kernel = lag_kernel(n_win * traces.shape[0])
    spectra = whiten(traces, quality)
    channels, parts, bins = spectra.shape
    half = parts // 2

    piece = lax.ppermute(spectra, ALL_AXES, column_permutation(n_chan, n_win))

    received = [spectra] + [
        lax.ppermute(spectra, "win", [(s, (s + shift) % n_win) for s in range(n_win)])
        for shift in range(1, n_win)
    ]
    mirrored = [received[(-m) % n_win] for m in range(n_win)]
    doubled = jnp.stack(mirrored + mirrored, axis=1)
    own = lax.dynamic_slice_in_dim(doubled, n_win - lax.axis_index("win"), n_win, axis=1)
    rotated = jnp.concatenate([own[:, :, half:], -own[:, :, :half]], axis=2)
    stacked = jnp.concatenate([own, rotated], axis=0).reshape(2 * channels, n_win * parts, bins)

    outs = []
    first = 0
    for size, order in STREAMS:
        theirs = gather_chan(piece[first:first + size], order)
        first += size
        theirs = theirs.reshape(n_win, per, size, parts, bins)
        theirs = jnp.transpose(theirs, (1, 2, 0, 3, 4)).reshape(per * size, n_win * parts, bins)
        cross = jnp.einsum(
            "iak,jak->ijk", stacked, theirs, preferred_element_type=jnp.float32
        ).astype(jnp.bfloat16)
        cross = cross.reshape(2, channels, per * size, bins)
        lags = jnp.einsum("pijk,pkt->ijt", cross, kernel, preferred_element_type=jnp.float32)
        outs.append(lags.astype(jnp.bfloat16).reshape(channels, per, size, LAGS))
    return jnp.concatenate(outs, axis=2).reshape(channels, per * channels, LAGS)


def solution(mesh):
    names = tuple(name for name, _ in CHAN_AXES)
    shape = tuple(size for _, size in CHAN_AXES) + (mesh.shape["win"],)
    fine = jax.sharding.Mesh(mesh.devices.reshape(shape), ALL_AXES)
    in_specs = (P("win", names, None), P("win", names))
    out_specs = P(names, "win", None)
    return jax.shard_map(body, mesh=fine, in_specs=in_specs, out_specs=out_specs, check_vma=False)
```

```python
import math

import jax
import jax.numpy as jnp
from jax import lax
from jax.sharding import PartitionSpec as P

SEGS = 8
NFFT = 256
F = 128
BAND = 8
LAGS = 128


epsilon = 1e-06


def forward_table():
    sample_index = jnp.arange(NFFT, dtype=jnp.int32)[:, None]
    bin_index = jnp.arange(1, F + 1, dtype=jnp.int32)[None, :]
    angles = 2.0 * jnp.pi / NFFT * (sample_index * bin_index % NFFT).astype(jnp.float32)
    norm_scale = 1.0 / math.sqrt(NFFT)
    return jnp.concatenate([jnp.cos(angles), -jnp.sin(angles)], axis=1) * norm_scale


def lag_kernel(window_total):
    bin_index = jnp.arange(1, F + 1, dtype=jnp.int32)[:, None]
    lag_shift = jnp.arange(LAGS, dtype=jnp.int32)[None, :] - LAGS // 2
    angles = 2.0 * jnp.pi / NFFT * (bin_index * lag_shift % NFFT).astype(jnp.float32)
    norm_scale = 2.0 / math.sqrt(F * SEGS * window_total)
    return jnp.stack([jnp.cos(angles) * norm_scale, -jnp.sin(angles) * norm_scale]).astype(
        jnp.bfloat16
    )


def whiten(traces, quality):
    win_count, channels = (traces.shape[0], traces.shape[1])
    segments = traces.reshape(win_count, channels, SEGS, NFFT)
    spectrum = jnp.dot(segments, forward_table(), precision=lax.Precision.HIGHEST)
    real_part = spectrum[..., :F]
    imag_part = spectrum[..., F:]
    power_sum = (real_part * real_part + imag_part * imag_part).reshape(
        win_count, channels, SEGS, F // BAND, BAND
    )
    amplitude = jnp.sqrt(jnp.mean(power_sum, axis=(2, 4)) + epsilon)
    factor = quality.astype(jnp.float32)[:, :, None] / amplitude
    factor = jnp.repeat(factor, BAND, axis=2)[:, :, None, :]
    stacked_parts = jnp.stack([real_part * factor, imag_part * factor], axis=0)
    stacked_parts = jnp.transpose(stacked_parts, (2, 0, 1, 3, 4)).reshape(
        channels, 2 * win_count * SEGS, F
    )
    return stacked_parts.astype(jnp.bfloat16)


def column_permutation(n_chan, n_win):
    per = n_chan // n_win
    return [
        (c * n_win + g, (per * g + c % per) * n_win + c // per)
        for c in range(n_chan)
        for g in range(n_win)
    ]


CHAN_AXES = (("z", 8), ("yh", 2), ("x", 4))
STREAMS = ((16, ("yh", "z", "x")), (16, ("yh", "x", "z")))
ALL_AXES = tuple(name for name, _ in CHAN_AXES) + ("win",)


def ring_all_gather(unit, axis, n):
    me = lax.axis_index(axis)
    blocks = [(0, unit)]
    if n == 2:
        blocks.append((1, lax.ppermute(unit, axis, [(0, 1), (1, 0)])))
    elif n > 2:
        up = [(i, (i + 1) % n) for i in range(n)]
        down = [(i, (i - 1) % n) for i in range(n)]
        forward = backward = unit
        for step in range(1, n // 2 + 1):
            if 2 * step < n:
                forward = lax.ppermute(forward, axis, up)
                backward = lax.ppermute(backward, axis, down)
                blocks += [(-step, forward), (step, backward)]
            else:
                half = unit.shape[-2] // 2
                first = lax.ppermute(forward[..., :half, :], axis, up)
                second = lax.ppermute(backward[..., half:, :], axis, down)
                blocks.append((step, jnp.concatenate([first, second], axis=-2)))
    buffer = jnp.zeros((n,) + unit.shape, unit.dtype)
    for offset, block in blocks:
        buffer = lax.dynamic_update_index_in_dim(buffer, block, (me + offset % n) % n, 0)
    return buffer


def gather_chan(unit, order):
    sizes = dict(CHAN_AXES)
    for axis in order:
        unit = ring_all_gather(unit, axis, sizes[axis])
    stages = list(reversed(order))
    perm = [stages.index(name) for name, _ in CHAN_AXES]
    return jnp.transpose(unit, perm + list(range(len(order), unit.ndim)))


def body(traces, quality):
    n_win = lax.axis_size("win")
    n_chan = 1
    for name, size in CHAN_AXES:
        n_chan *= size
    per = n_chan // n_win
    kernel = lag_kernel(n_win * traces.shape[0])
    spectra = whiten(traces, quality)
    channels, parts, bins = spectra.shape
    half = parts // 2

    piece = lax.ppermute(spectra, ALL_AXES, column_permutation(n_chan, n_win))

    received = [spectra] + [
        lax.ppermute(spectra, "win", [(s, (s + shift) % n_win) for s in range(n_win)])
        for shift in range(1, n_win)
    ]
    mirrored = [received[(-m) % n_win] for m in range(n_win)]
    doubled = jnp.stack(mirrored + mirrored, axis=1)
    own = lax.dynamic_slice_in_dim(doubled, n_win - lax.axis_index("win"), n_win, axis=1)
    rotated = jnp.concatenate([own[:, :, half:], -own[:, :, :half]], axis=2)
    stacked = jnp.concatenate([own, rotated], axis=0)

    outs = []
    first = 0
    for size, order in STREAMS:
        theirs = gather_chan(piece[first:first + size], order)
        first += size
        theirs = theirs.reshape(n_win, per * size, parts, bins)
        cross = jnp.einsum(
            "igak,gjak->ijk", stacked, theirs, preferred_element_type=jnp.float32
        ).astype(jnp.bfloat16)
        cross = cross.reshape(2, channels, per * size, bins)
        lags = jnp.einsum("pijk,pkt->ijt", cross, kernel, preferred_element_type=jnp.float32)
        outs.append(lags.astype(jnp.bfloat16).reshape(channels, per, size, LAGS))
    return jnp.concatenate(outs, axis=2).reshape(channels, per * channels, LAGS)


def solution(mesh):
    names = tuple(name for name, _ in CHAN_AXES)
    shape = tuple(size for _, size in CHAN_AXES) + (mesh.shape["win"],)
    fine = jax.sharding.Mesh(mesh.devices.reshape(shape), ALL_AXES)
    in_specs = (P("win", names, None), P("win", names))
    out_specs = P(names, "win", None)
    return jax.shard_map(body, mesh=fine, in_specs=in_specs, out_specs=out_specs, check_vma=False)
```

```python
import math

import jax
import jax.numpy as jnp
from jax import lax
from jax.sharding import PartitionSpec as P

SEGS = 8
NFFT = 256
F = 128
BAND = 8
LAGS = 128


epsilon = 1e-06


def forward_table():
    sample_index = jnp.arange(NFFT, dtype=jnp.int32)[:, None]
    bin_index = jnp.arange(1, F + 1, dtype=jnp.int32)[None, :]
    angles = 2.0 * jnp.pi / NFFT * (sample_index * bin_index % NFFT).astype(jnp.float32)
    norm_scale = 1.0 / math.sqrt(NFFT)
    return jnp.concatenate([jnp.cos(angles), -jnp.sin(angles)], axis=1) * norm_scale


def lag_kernel(window_total):
    bin_index = jnp.arange(1, F + 1, dtype=jnp.int32)[:, None]
    lag_shift = jnp.arange(LAGS, dtype=jnp.int32)[None, :] - LAGS // 2
    angles = 2.0 * jnp.pi / NFFT * (bin_index * lag_shift % NFFT).astype(jnp.float32)
    norm_scale = 2.0 / math.sqrt(F * SEGS * window_total)
    return jnp.stack([jnp.cos(angles) * norm_scale, -jnp.sin(angles) * norm_scale]).astype(
        jnp.bfloat16
    )


def whiten(traces, quality):
    win_count, channels = (traces.shape[0], traces.shape[1])
    segments = traces.reshape(win_count, channels, SEGS, NFFT)
    spectrum = jnp.dot(segments, forward_table(), precision=lax.Precision.HIGHEST)
    real_part = spectrum[..., :F]
    imag_part = spectrum[..., F:]
    power_sum = (real_part * real_part + imag_part * imag_part).reshape(
        win_count, channels, SEGS, F // BAND, BAND
    )
    amplitude = jnp.sqrt(jnp.mean(power_sum, axis=(2, 4)) + epsilon)
    factor = quality.astype(jnp.float32)[:, :, None] / amplitude
    factor = jnp.repeat(factor, BAND, axis=2)[:, :, None, :]
    stacked_parts = jnp.stack([real_part * factor, imag_part * factor], axis=0)
    stacked_parts = jnp.transpose(stacked_parts, (2, 0, 1, 3, 4)).reshape(
        channels, 2 * win_count * SEGS, F
    )
    return stacked_parts.astype(jnp.bfloat16)


def column_permutation(n_chan, n_win):
    per = n_chan // n_win
    return [
        (c * n_win + g, (per * g + c % per) * n_win + c // per)
        for c in range(n_chan)
        for g in range(n_win)
    ]


CHAN_AXES = (("z", 8), ("yh", 2), ("x", 4))
STREAMS = ((16, ("yh", "z", "x")), (16, ("yh", "x", "z")))
ALL_AXES = tuple(name for name, _ in CHAN_AXES) + ("win",)


def ring_all_gather(unit, axis, n, final=False):
    me = lax.axis_index(axis)
    blocks = [(0, unit)]
    if n == 2:
        blocks.append((1, lax.ppermute(unit, axis, [(0, 1), (1, 0)])))
    elif n > 2:
        up = [(i, (i + 1) % n) for i in range(n)]
        down = [(i, (i - 1) % n) for i in range(n)]
        forward = backward = unit
        for step in range(1, n // 2 + 1):
            if 2 * step < n or not final:
                forward = lax.ppermute(forward, axis, up)
                if 2 * step == n:
                    blocks.append((-step, forward))
                    break
                backward = lax.ppermute(backward, axis, down)
                blocks += [(-step, forward), (step, backward)]
            else:
                half = unit.shape[-2] // 2
                first = lax.ppermute(forward[..., :half, :], axis, up)
                second = lax.ppermute(backward[..., half:, :], axis, down)
                blocks.append((step, jnp.concatenate([first, second], axis=-2)))
    buffer = jnp.zeros((n,) + unit.shape, unit.dtype)
    for offset, block in blocks:
        buffer = lax.dynamic_update_index_in_dim(buffer, block, (me + offset % n) % n, 0)
    return buffer


def gather_chan(unit, order):
    sizes = dict(CHAN_AXES)
    for number, axis in enumerate(order):
        unit = ring_all_gather(unit, axis, sizes[axis], final=number == len(order) - 1)
    stages = list(reversed(order))
    perm = [stages.index(name) for name, _ in CHAN_AXES]
    return jnp.transpose(unit, perm + list(range(len(order), unit.ndim)))


def body(traces, quality):
    n_win = lax.axis_size("win")
    n_chan = 1
    for name, size in CHAN_AXES:
        n_chan *= size
    per = n_chan // n_win
    kernel = lag_kernel(n_win * traces.shape[0])
    spectra = whiten(traces, quality)
    channels, parts, bins = spectra.shape
    half = parts // 2

    piece = lax.ppermute(spectra, ALL_AXES, column_permutation(n_chan, n_win))

    received = [spectra] + [
        lax.ppermute(spectra, "win", [(s, (s + shift) % n_win) for s in range(n_win)])
        for shift in range(1, n_win)
    ]
    mirrored = [received[(-m) % n_win] for m in range(n_win)]
    doubled = jnp.stack(mirrored + mirrored, axis=1)
    own = lax.dynamic_slice_in_dim(doubled, n_win - lax.axis_index("win"), n_win, axis=1)
    rotated = jnp.concatenate([own[:, :, half:], -own[:, :, :half]], axis=2)
    stacked = jnp.concatenate([own, rotated], axis=0)

    outs = []
    first = 0
    for size, order in STREAMS:
        theirs = gather_chan(piece[first:first + size], order)
        first += size
        theirs = theirs.reshape(n_win, per * size, parts, bins)
        cross = jnp.einsum(
            "igak,gjak->ijk", stacked, theirs, preferred_element_type=jnp.float32
        ).astype(jnp.bfloat16)
        cross = cross.reshape(2, channels, per * size, bins)
        lags = jnp.einsum("pijk,pkt->ijt", cross, kernel, preferred_element_type=jnp.float32)
        outs.append(lags.astype(jnp.bfloat16).reshape(channels, per, size, LAGS))
    return jnp.concatenate(outs, axis=2).reshape(channels, per * channels, LAGS)


def solution(mesh):
    names = tuple(name for name, _ in CHAN_AXES)
    shape = tuple(size for _, size in CHAN_AXES) + (mesh.shape["win"],)
    fine = jax.sharding.Mesh(mesh.devices.reshape(shape), ALL_AXES)
    in_specs = (P("win", names, None), P("win", names))
    out_specs = P(names, "win", None)
    return jax.shard_map(body, mesh=fine, in_specs=in_specs, out_specs=out_specs, check_vma=False)
```

```python
import math

import jax
import jax.numpy as jnp
from jax import lax
from jax.sharding import PartitionSpec as P

SEGS = 8
NFFT = 256
F = 128
BAND = 8
LAGS = 128


epsilon = 1e-06


def forward_table():
    sample_index = jnp.arange(NFFT, dtype=jnp.int32)[:, None]
    bin_index = jnp.arange(1, F + 1, dtype=jnp.int32)[None, :]
    angles = 2.0 * jnp.pi / NFFT * (sample_index * bin_index % NFFT).astype(jnp.float32)
    norm_scale = 1.0 / math.sqrt(NFFT)
    return jnp.concatenate([jnp.cos(angles), -jnp.sin(angles)], axis=1) * norm_scale


def lag_kernel(window_total):
    bin_index = jnp.arange(1, F + 1, dtype=jnp.int32)[:, None]
    lag_shift = jnp.arange(LAGS, dtype=jnp.int32)[None, :] - LAGS // 2
    angles = 2.0 * jnp.pi / NFFT * (bin_index * lag_shift % NFFT).astype(jnp.float32)
    norm_scale = 2.0 / math.sqrt(F * SEGS * window_total)
    return jnp.stack([jnp.cos(angles) * norm_scale, -jnp.sin(angles) * norm_scale]).astype(
        jnp.bfloat16
    )


def whiten(traces, quality):
    win_count, channels = (traces.shape[0], traces.shape[1])
    segments = traces.reshape(win_count, channels, SEGS, NFFT)
    spectrum = jnp.dot(segments, forward_table(), precision=lax.Precision.HIGHEST)
    real_part = spectrum[..., :F]
    imag_part = spectrum[..., F:]
    power_sum = (real_part * real_part + imag_part * imag_part).reshape(
        win_count, channels, SEGS, F // BAND, BAND
    )
    amplitude = jnp.sqrt(jnp.mean(power_sum, axis=(2, 4)) + epsilon)
    factor = quality.astype(jnp.float32)[:, :, None] / amplitude
    factor = jnp.repeat(factor, BAND, axis=2)[:, :, None, :]
    stacked_parts = jnp.stack([real_part * factor, imag_part * factor], axis=0)
    stacked_parts = jnp.transpose(stacked_parts, (2, 0, 1, 3, 4)).reshape(
        channels, 2 * win_count * SEGS, F
    )
    return stacked_parts.astype(jnp.bfloat16)


def column_permutation(n_chan, n_win):
    per = n_chan // n_win
    return [
        (c * n_win + g, (per * g + c % per) * n_win + c // per)
        for c in range(n_chan)
        for g in range(n_win)
    ]


CHAN_AXES = (("z", 8), ("yh", 2), ("x", 4))
STREAMS = ((16, ("z", "x")), (16, ("x", "z")))
ALL_AXES = tuple(name for name, _ in CHAN_AXES) + ("win",)


def ring_all_gather(unit, axis, n):
    me = lax.axis_index(axis)
    blocks = [(0, unit)]
    if n == 2:
        blocks.append((1, lax.ppermute(unit, axis, [(0, 1), (1, 0)])))
    elif n > 2:
        up = [(i, (i + 1) % n) for i in range(n)]
        down = [(i, (i - 1) % n) for i in range(n)]
        forward = backward = unit
        for step in range(1, n // 2 + 1):
            if 2 * step < n:
                forward = lax.ppermute(forward, axis, up)
                backward = lax.ppermute(backward, axis, down)
                blocks += [(-step, forward), (step, backward)]
            else:
                half = unit.shape[-2] // 2
                first = lax.ppermute(forward[..., :half, :], axis, up)
                second = lax.ppermute(backward[..., half:, :], axis, down)
                blocks.append((step, jnp.concatenate([first, second], axis=-2)))
    buffer = jnp.zeros((n,) + unit.shape, unit.dtype)
    for offset, block in blocks:
        buffer = lax.dynamic_update_index_in_dim(buffer, block, (me + offset % n) % n, 0)
    return buffer


def gather_chan(unit, order, done):
    sizes = dict(CHAN_AXES)
    for axis in order:
        unit = ring_all_gather(unit, axis, sizes[axis])
    stages = list(reversed(order)) + list(done)
    perm = [stages.index(name) for name, _ in CHAN_AXES]
    return jnp.transpose(unit, perm + list(range(len(stages), unit.ndim)))


def body(traces, quality):
    n_win = lax.axis_size("win")
    n_chan = 1
    for name, size in CHAN_AXES:
        n_chan *= size
    per = n_chan // n_win
    kernel = lag_kernel(n_win * traces.shape[0])
    spectra = whiten(traces, quality)
    channels, parts, bins = spectra.shape
    half = parts // 2

    sizes = dict(CHAN_AXES)
    stride = sizes["x"] * n_win
    moves = column_permutation(n_chan, n_win)
    piece = lax.ppermute(spectra, ALL_AXES, moves)
    partner = lax.ppermute(
        spectra, ALL_AXES, [(src, dst ^ stride) for src, dst in moves]
    )
    yh = lax.axis_index("yh")
    shared = jnp.stack([piece, partner])
    shared = jnp.where(yh == 0, shared, shared[::-1])

    received = [spectra] + [
        lax.ppermute(spectra, "win", [(s, (s + shift) % n_win) for s in range(n_win)])
        for shift in range(1, n_win)
    ]
    mirrored = [received[(-m) % n_win] for m in range(n_win)]
    doubled = jnp.stack(mirrored + mirrored, axis=1)
    own = lax.dynamic_slice_in_dim(doubled, n_win - lax.axis_index("win"), n_win, axis=1)
    rotated = jnp.concatenate([own[:, :, half:], -own[:, :, :half]], axis=2)
    stacked = jnp.concatenate([own, rotated], axis=0).reshape(2 * channels, n_win * parts, bins)

    outs = []
    first = 0
    for size, order in STREAMS:
        theirs = gather_chan(shared[:, first:first + size], order, ["yh"])
        first += size
        theirs = theirs.reshape(n_win, per, size, parts, bins)
        theirs = jnp.transpose(theirs, (1, 2, 0, 3, 4)).reshape(per * size, n_win * parts, bins)
        cross = jnp.einsum(
            "iak,jak->ijk", stacked, theirs, preferred_element_type=jnp.float32
        ).astype(jnp.bfloat16)
        cross = cross.reshape(2, channels, per * size, bins)
        lags = jnp.einsum("pijk,pkt->ijt", cross, kernel, preferred_element_type=jnp.float32)
        outs.append(lags.astype(jnp.bfloat16).reshape(channels, per, size, LAGS))
    return jnp.concatenate(outs, axis=2).reshape(channels, per * channels, LAGS)


def solution(mesh):
    names = tuple(name for name, _ in CHAN_AXES)
    shape = tuple(size for _, size in CHAN_AXES) + (mesh.shape["win"],)
    fine = jax.sharding.Mesh(mesh.devices.reshape(shape), ALL_AXES)
    in_specs = (P("win", names, None), P("win", names))
    out_specs = P(names, "win", None)
    return jax.shard_map(body, mesh=fine, in_specs=in_specs, out_specs=out_specs, check_vma=False)
```

```python
import math

import jax
import jax.numpy as jnp
from jax import lax
from jax.sharding import PartitionSpec as P

SEGS = 8
NFFT = 256
F = 128
BAND = 8
LAGS = 128


epsilon = 1e-06


def forward_table():
    sample_index = jnp.arange(NFFT, dtype=jnp.int32)[:, None]
    bin_index = jnp.arange(1, F + 1, dtype=jnp.int32)[None, :]
    angles = 2.0 * jnp.pi / NFFT * (sample_index * bin_index % NFFT).astype(jnp.float32)
    norm_scale = 1.0 / math.sqrt(NFFT)
    return jnp.concatenate([jnp.cos(angles), -jnp.sin(angles)], axis=1) * norm_scale


def lag_kernel(window_total):
    bin_index = jnp.arange(1, F + 1, dtype=jnp.int32)[:, None]
    lag_shift = jnp.arange(LAGS, dtype=jnp.int32)[None, :] - LAGS // 2
    angles = 2.0 * jnp.pi / NFFT * (bin_index * lag_shift % NFFT).astype(jnp.float32)
    norm_scale = 2.0 / math.sqrt(F * SEGS * window_total)
    return jnp.stack([jnp.cos(angles) * norm_scale, -jnp.sin(angles) * norm_scale]).astype(
        jnp.bfloat16
    )


def whiten(traces, quality):
    win_count, channels = (traces.shape[0], traces.shape[1])
    segments = traces.reshape(win_count, channels, SEGS, NFFT)
    spectrum = jnp.dot(segments, forward_table(), precision=lax.Precision.HIGHEST)
    real_part = spectrum[..., :F]
    imag_part = spectrum[..., F:]
    power_sum = (real_part * real_part + imag_part * imag_part).reshape(
        win_count, channels, SEGS, F // BAND, BAND
    )
    amplitude = jnp.sqrt(jnp.mean(power_sum, axis=(2, 4)) + epsilon)
    factor = quality.astype(jnp.float32)[:, :, None] / amplitude
    factor = jnp.repeat(factor, BAND, axis=2)[:, :, None, :]
    stacked_parts = jnp.stack([real_part * factor, imag_part * factor], axis=0)
    stacked_parts = jnp.transpose(stacked_parts, (2, 0, 1, 3, 4)).reshape(
        channels, 2 * win_count * SEGS, F
    )
    return stacked_parts.astype(jnp.bfloat16)


def column_permutation(n_chan, n_win):
    per = n_chan // n_win
    return [
        (c * n_win + g, (per * g + c % per) * n_win + c // per)
        for c in range(n_chan)
        for g in range(n_win)
    ]


CHAN_AXES = (("z", 8), ("yh", 2), ("x", 4))
STREAMS = ((16, ("yh", "z", "x")), (16, ("yh", "x", "z")))
ALL_AXES = tuple(name for name, _ in CHAN_AXES) + ("win",)


def ring_all_gather(unit, axis, n):
    me = lax.axis_index(axis)
    blocks = [(0, unit)]
    if n == 2:
        blocks.append((1, lax.ppermute(unit, axis, [(0, 1), (1, 0)])))
    elif n > 2:
        up = [(i, (i + 1) % n) for i in range(n)]
        down = [(i, (i - 1) % n) for i in range(n)]
        forward = backward = unit
        for step in range(1, n // 2 + 1):
            if 2 * step < n:
                forward = lax.ppermute(forward, axis, up)
                backward = lax.ppermute(backward, axis, down)
                blocks += [(-step, forward), (step, backward)]
            else:
                half = unit.shape[-2] // 2
                first = lax.ppermute(forward[..., :half, :], axis, up)
                second = lax.ppermute(backward[..., half:, :], axis, down)
                blocks.append((step, jnp.concatenate([first, second], axis=-2)))
    buffer = jnp.zeros((n,) + unit.shape, unit.dtype)
    for offset, block in blocks:
        buffer = lax.dynamic_update_index_in_dim(buffer, block, (me + offset % n) % n, 0)
    return buffer


def gather_chan(unit, order):
    sizes = dict(CHAN_AXES)
    for axis in order:
        unit = ring_all_gather(unit, axis, sizes[axis])
    stages = list(reversed(order))
    perm = [stages.index(name) for name, _ in CHAN_AXES]
    return jnp.transpose(unit, perm + list(range(len(order), unit.ndim)))


def body(traces, quality):
    n_win = lax.axis_size("win")
    n_chan = 1
    for name, size in CHAN_AXES:
        n_chan *= size
    per = n_chan // n_win
    kernel = lag_kernel(n_win * traces.shape[0])
    spectra = whiten(traces, quality)
    channels, parts, bins = spectra.shape
    half = parts // 2

    piece = lax.ppermute(spectra, ALL_AXES, column_permutation(n_chan, n_win))

    received = [spectra] + [
        lax.ppermute(spectra, "win", [(s, (s + shift) % n_win) for s in range(n_win)])
        for shift in range(1, n_win)
    ]
    mirrored = [received[(-m) % n_win] for m in range(n_win)]
    doubled = jnp.stack(mirrored + mirrored, axis=1)
    own = lax.dynamic_slice_in_dim(doubled, n_win - lax.axis_index("win"), n_win, axis=1)
    rotated = jnp.concatenate([own[:, :, half:], -own[:, :, :half]], axis=2)
    stacked = jnp.concatenate([own, rotated], axis=0)

    starts = []
    first = 0
    for size, order in STREAMS:
        starts.append(first)
        first += size
    outs = [None] * len(STREAMS)
    earlier = None
    for index in sorted(range(len(STREAMS)), key=lambda s: STREAMS[s][1][-1] != "z"):
        size, order = STREAMS[index]
        first = starts[index]
        theirs = gather_chan(piece[first:first + size], order)
        if earlier is not None:
            earlier, theirs = lax.optimization_barrier((earlier, theirs))
            outs[previous] = earlier
        theirs = theirs.reshape(n_win, per * size, parts, bins)
        cross = jnp.einsum(
            "igak,gjak->ijk", stacked, theirs, preferred_element_type=jnp.float32
        ).astype(jnp.bfloat16)
        cross = cross.reshape(2, channels, per * size, bins)
        lags = jnp.einsum("pijk,pkt->ijt", cross, kernel, preferred_element_type=jnp.float32)
        outs[index] = lags.astype(jnp.bfloat16).reshape(channels, per, size, LAGS)
        earlier, previous = outs[index], index
    return jnp.concatenate(outs, axis=2).reshape(channels, per * channels, LAGS)


def solution(mesh):
    names = tuple(name for name, _ in CHAN_AXES)
    shape = tuple(size for _, size in CHAN_AXES) + (mesh.shape["win"],)
    fine = jax.sharding.Mesh(mesh.devices.reshape(shape), ALL_AXES)
    in_specs = (P("win", names, None), P("win", names))
    out_specs = P(names, "win", None)
    return jax.shard_map(body, mesh=fine, in_specs=in_specs, out_specs=out_specs, check_vma=False)
```

```python
import math

import jax
import jax.numpy as jnp
from jax import lax
from jax.sharding import PartitionSpec as P

SEGS = 8
NFFT = 256
F = 128
BAND = 8
LAGS = 128


epsilon = 1e-06


def forward_table():
    sample_index = jnp.arange(NFFT, dtype=jnp.int32)[:, None]
    bin_index = jnp.arange(1, F + 1, dtype=jnp.int32)[None, :]
    angles = 2.0 * jnp.pi / NFFT * (sample_index * bin_index % NFFT).astype(jnp.float32)
    norm_scale = 1.0 / math.sqrt(NFFT)
    return jnp.concatenate([jnp.cos(angles), -jnp.sin(angles)], axis=1) * norm_scale


def lag_kernel(window_total):
    bin_index = jnp.arange(1, F + 1, dtype=jnp.int32)[:, None]
    lag_shift = jnp.arange(LAGS, dtype=jnp.int32)[None, :] - LAGS // 2
    angles = 2.0 * jnp.pi / NFFT * (bin_index * lag_shift % NFFT).astype(jnp.float32)
    norm_scale = 2.0 / math.sqrt(F * SEGS * window_total)
    return jnp.stack([jnp.cos(angles) * norm_scale, -jnp.sin(angles) * norm_scale]).astype(
        jnp.bfloat16
    )


def whiten(traces, quality):
    win_count, channels = (traces.shape[0], traces.shape[1])
    segments = traces.reshape(win_count, channels, SEGS, NFFT)
    spectrum = jnp.dot(segments, forward_table(), precision=lax.Precision.HIGHEST)
    real_part = spectrum[..., :F]
    imag_part = spectrum[..., F:]
    power_sum = (real_part * real_part + imag_part * imag_part).reshape(
        win_count, channels, SEGS, F // BAND, BAND
    )
    amplitude = jnp.sqrt(jnp.mean(power_sum, axis=(2, 4)) + epsilon)
    factor = quality.astype(jnp.float32)[:, :, None] / amplitude
    factor = jnp.repeat(factor, BAND, axis=2)[:, :, None, :]
    stacked_parts = jnp.stack([real_part * factor, imag_part * factor], axis=0)
    stacked_parts = jnp.transpose(stacked_parts, (2, 0, 1, 3, 4)).reshape(
        channels, 2 * win_count * SEGS, F
    )
    return stacked_parts.astype(jnp.bfloat16)


def column_permutation(n_chan, n_win):
    per = n_chan // n_win
    return [
        (c * n_win + g, (per * g + c % per) * n_win + c // per)
        for c in range(n_chan)
        for g in range(n_win)
    ]


CHAN_AXES = (("z", 8), ("yh", 2), ("x", 4))
STREAMS = ((12, ("yh", "z", "x")), (20, ("yh", "x", "z")))
ALL_AXES = tuple(name for name, _ in CHAN_AXES) + ("win",)


def ring_all_gather(unit, axis, n):
    me = lax.axis_index(axis)
    blocks = [(0, unit)]
    if n == 2:
        blocks.append((1, lax.ppermute(unit, axis, [(0, 1), (1, 0)])))
    elif n > 2:
        up = [(i, (i + 1) % n) for i in range(n)]
        down = [(i, (i - 1) % n) for i in range(n)]
        forward = backward = unit
        for step in range(1, n // 2 + 1):
            if 2 * step < n:
                forward = lax.ppermute(forward, axis, up)
                backward = lax.ppermute(backward, axis, down)
                blocks += [(-step, forward), (step, backward)]
            else:
                half = unit.shape[-2] // 2
                first = lax.ppermute(forward[..., :half, :], axis, up)
                second = lax.ppermute(backward[..., half:, :], axis, down)
                blocks.append((step, jnp.concatenate([first, second], axis=-2)))
    buffer = jnp.zeros((n,) + unit.shape, unit.dtype)
    for offset, block in blocks:
        buffer = lax.dynamic_update_index_in_dim(buffer, block, (me + offset % n) % n, 0)
    return buffer


def gather_chan(unit, order):
    sizes = dict(CHAN_AXES)
    for axis in order:
        unit = ring_all_gather(unit, axis, sizes[axis])
    stages = list(reversed(order))
    perm = [stages.index(name) for name, _ in CHAN_AXES]
    return jnp.transpose(unit, perm + list(range(len(order), unit.ndim)))


def body(traces, quality):
    n_win = lax.axis_size("win")
    n_chan = 1
    for name, size in CHAN_AXES:
        n_chan *= size
    per = n_chan // n_win
    kernel = lag_kernel(n_win * traces.shape[0])
    spectra = whiten(traces, quality)
    channels, parts, bins = spectra.shape
    half = parts // 2

    piece = lax.ppermute(spectra, ALL_AXES, column_permutation(n_chan, n_win))

    received = [spectra] + [
        lax.ppermute(spectra, "win", [(s, (s + shift) % n_win) for s in range(n_win)])
        for shift in range(1, n_win)
    ]
    mirrored = [received[(-m) % n_win] for m in range(n_win)]
    doubled = jnp.stack(mirrored + mirrored, axis=1)
    own = lax.dynamic_slice_in_dim(doubled, n_win - lax.axis_index("win"), n_win, axis=1)
    rotated = jnp.concatenate([own[:, :, half:], -own[:, :, :half]], axis=2)
    stacked = jnp.concatenate([own, rotated], axis=0)

    starts = []
    first = 0
    for size, order in STREAMS:
        starts.append(first)
        first += size
    outs = [None] * len(STREAMS)
    earlier = None
    for index in sorted(range(len(STREAMS)), key=lambda s: STREAMS[s][1][-1] != "z"):
        size, order = STREAMS[index]
        first = starts[index]
        theirs = gather_chan(piece[first:first + size], order)
        if earlier is not None:
            earlier, theirs = lax.optimization_barrier((earlier, theirs))
            outs[previous] = earlier
        theirs = theirs.reshape(n_win, per * size, parts, bins)
        cross = jnp.einsum(
            "igak,gjak->ijk", stacked, theirs, preferred_element_type=jnp.float32
        ).astype(jnp.bfloat16)
        cross = cross.reshape(2, channels, per * size, bins)
        lags = jnp.einsum("pijk,pkt->ijt", cross, kernel, preferred_element_type=jnp.float32)
        outs[index] = lags.astype(jnp.bfloat16).reshape(channels, per, size, LAGS)
        earlier, previous = outs[index], index
    return jnp.concatenate(outs, axis=2).reshape(channels, per * channels, LAGS)


def solution(mesh):
    names = tuple(name for name, _ in CHAN_AXES)
    shape = tuple(size for _, size in CHAN_AXES) + (mesh.shape["win"],)
    fine = jax.sharding.Mesh(mesh.devices.reshape(shape), ALL_AXES)
    in_specs = (P("win", names, None), P("win", names))
    out_specs = P(names, "win", None)
    return jax.shard_map(body, mesh=fine, in_specs=in_specs, out_specs=out_specs, check_vma=False)
```
